768 devices in a mesh: wall: 16 (over y_hi, x), normal: 48 (over y_lo, z, core).
Axes of the slice: x: 4, y: 8 (y_hi: 4, y_lo: 2; y = y_hi * 2 + y_lo), z: 12, core: 2. Of those that a mesh axis runs over, the one named last changes fastest.
Arguments:
- profiles: float32 [3, 64, 32, 18432], P(None, None, 'wall', 'normal'), may hold values from -6 to 6
- plane: float32 [3, 128, 49152], P(None, 'wall', 'normal'), may hold values from -6 to 6
- match_cell: int32 [32, 18432], P('wall', 'normal'), may hold values from 0 to 393215, as said below
- burning: int32 [32, 18432], P('wall', 'normal'), may hold values 0 or 1
Outputs:
- new_profiles: float32 [3, 64, 32, 18432], P(None, None, 'wall', 'normal')
- wall_flux: float32 [3, 128, 49152], P(None, 'wall', 'normal')
The draws below stay inside these ranges and needn't reach their ends.
Inputs may be any that keep to these rules, and one draw needn't show every extreme that they name: `match_cell`: read in row-major order, the faces of one device fall into 48 runs of 16; run j names only cells of block column j and of the same block row: m = j * 8 * 1024 + row * 1024 + column.
All inputs are finite; a program needn't handle non-finite values. No bound on the sum of `burning` on one device may be relied on, other than what follows from the above.
Results may differ from the reference program's by a relative error of at most 0.000071.
Values sent between devices are 32-bit elements; how exact they have to be, the bound alone decides.
No kernel may reach another device: no remote copies, remote signals or barrier semaphores. Data moves between devices by JAX's collectives and lax.ppermute only.
A program may use at most 32 MiB of HBM per device.

```python
import jax
import jax.numpy as jnp
import numpy as np
from jax import lax

NP = 64
FR = 2
FC = 384
GW = 8
GN = 1024
NR = 32
NC = 18432
N_WALL = 16
N_NORMAL = 48


def draw_match_cell(key, part):
    row_local = (jnp.arange(NR, dtype=jnp.int32) % FR)[:, None]
    col_local = (jnp.arange(NC, dtype=jnp.int32) % FC)[None, :]
    flat_index = row_local * FC + col_local
    source_peer = flat_index // (FR * FC // N_NORMAL)
    local_cell = jax.random.randint(key, (NR, NC), 0, GW * GN, dtype=jnp.int32)
    return source_peer * (GW * GN) + local_cell


def set_ends(result, stream_key, smallest, high):
    index_at = [jax.random.randint(jax.random.fold_in(stream_key, axis), (), 0, length) for axis, length in enumerate(result.shape)]
    main_axis = result.shape.index(max(result.shape))
    neighbour = index_at[:main_axis] + [(index_at[main_axis] + 1) % result.shape[main_axis]] + index_at[main_axis + 1:]
    return result.at[tuple(index_at)].set(smallest).at[tuple(neighbour)].set(high)


def level_of(stream_key, extent, pieces, smallest, largest):
    def one(dim, parts):
        steps = jax.random.uniform(jax.random.fold_in(jax.random.fold_in(stream_key, 6), dim), (parts,), jnp.float32, smallest / len(pieces), largest / len(pieces))
        return jnp.repeat(jnp.exp(steps), extent[dim] // parts).reshape((-1,) + (1,) * (len(extent) - dim - 1))

    level = one(*pieces[0])
    for cut in pieces[1:]:
        level = level * one(*cut)
    return level


def gaussian(stream_key, shape, width, limit, cuts=(), held_as=jnp.bfloat16):
    result = width * jax.random.normal(stream_key, shape, jnp.float32)
    if cuts:
        result = result * level_of(stream_key, shape, cuts, -0.22, 0.18)
    return jnp.clip(result, -limit, limit).astype(held_as)


def setup_inputs(seed: int = 0) -> dict:
    arg_keys = jax.random.split(jax.random.key(seed), 5)
    profiles = gaussian(arg_keys[0], (3, NP, NR, NC), 1.0, 6.0, ((2, 16), (3, 48)), jnp.float32)
    plane = gaussian(arg_keys[1], (3, GW * N_WALL, GN * N_NORMAL), 1.0, 6.0, ((1, 16), (2, 48)), jnp.float32)
    match_cell = draw_match_cell(jax.random.fold_in(arg_keys[4], 71), 0)
    burning = set_ends((jax.random.randint(arg_keys[3], (NR, NC), 0, 4) < 1).astype(jnp.int32), jax.random.fold_in(arg_keys[3], 1), 0, 1)
    return {"profiles": profiles, "plane": plane, "match_cell": match_cell, "burning": burning}


visc_base = 0.001
mix_coef = 1e-05
prandtl = 0.7
burn_rate = 15000.0
lateral_coef = 4000.0
step_size = 2e-05

def cheb_matrix(points):
    indices = np.arange(points)
    heights = (1.0 - np.cos(np.pi * indices / (points - 1))) / 2.0
    weights = np.where(indices % 2 == 0, 1.0, -1.0)
    weights[0] = weights[0] * 0.5
    weights[-1] = weights[-1] * 0.5
    identity = np.eye(points)
    spacing = heights[:, None] - heights[None, :] + identity
    matrix = weights[None, :] / weights[:, None] / spacing
    matrix = np.where(identity > 0.5, 0.0, matrix)
    matrix = matrix - identity * matrix.sum(axis=1)[:, None]
    return (matrix.astype(np.float32), heights.astype(np.float32))

def set_bounds(profiles, matched):
    point = jnp.arange(profiles.shape[1])[None, :, None, None]
    state = jnp.where(point == profiles.shape[1] - 1, matched[:, None], profiles)
    return jnp.where(point == 0, jnp.float32(0.0), state)

def advance(state, padded, burning, deriv, heights):
    grad = jnp.einsum('ij,kjrc->kirc', deriv, state, precision=lax.Precision.HIGHEST)
    shear = jnp.sqrt(grad[0] * grad[0] + grad[1] * grad[1] + 1e-06)
    visc = visc_base + mix_coef * (heights * heights)[:, None, None] * shear
    scales = jnp.array([1.0, 1.0, 1.0 / prandtl], jnp.float32)[:, None, None, None]
    diffusion = jnp.einsum('ij,kjrc->kirc', deriv, visc[None] * scales * grad, precision=lax.Precision.HIGHEST)
    lateral = padded[:, :, 2:] + padded[:, :, :-2] - 2.0 * state
    source = burn_rate * jnp.exp(-heights / 0.15)[:, None, None] * burning.astype(jnp.float32)[None]
    tendency = diffusion + lateral_coef * lateral
    tendency = tendency.at[2].add(source)
    point = jnp.arange(state.shape[1])
    interior = ((point > 0) & (point < state.shape[1] - 1))[None, :, None, None]
    new_state = jnp.where(interior, state + step_size * tendency, state)
    stress = visc_base * scales[:, 0] * jnp.einsum('j,kjrc->krc', deriv[0], new_state, precision=lax.Precision.HIGHEST)
    return (new_state, stress)

def reference(profiles, plane, match_cell, burning):
    deriv_np, height_np = cheb_matrix(NP)
    deriv = jnp.asarray(deriv_np, jnp.float32)
    heights = jnp.asarray(height_np, jnp.float32)
    cell_count = GW * GN
    row_wall = (jnp.arange(NR, dtype=jnp.int32) // FR)[:, None]
    source_peer = match_cell // cell_count
    local_cell = match_cell % cell_count
    plane_row = (row_wall * GW + local_cell // GN).astype(jnp.int32)
    plane_col = (source_peer * GN + local_cell % GN).astype(jnp.int32)
    matched = plane[:, plane_row, plane_col]
    state = set_bounds(profiles, matched)
    padded = jnp.pad(state, ((0, 0), (0, 0), (1, 1), (0, 0)))
    new_state, stress = advance(state, padded, burning, deriv, heights)
    wall_flux = jnp.zeros_like(plane).at[:, plane_row, plane_col].add(stress)
    return (new_state, wall_flux)
```

```python
import jax
import jax.numpy as jnp
import numpy as np
from jax import lax
from jax.sharding import PartitionSpec as P

visc_base = 0.001
mix_coef = 1e-05
prandtl = 0.7
burn_rate = 15000.0
lateral_coef = 4000.0
step_size = 2e-05


def padded_2(cells, sides, width):
    for axis, dim in sides:
        count = lax.axis_size(axis)
        ends = count - 1
        head = lax.slice_in_dim(cells, 0, width, axis=dim)
        tail = lax.slice_in_dim(cells, cells.shape[dim] - width, cells.shape[dim], axis=dim)
        cells = jnp.concatenate(
            [
                lax.ppermute(tail, axis, [(i, (i + 1) % count) for i in range(ends)]),
                cells,
                lax.ppermute(head, axis, [((i + 1) % count, i) for i in range(ends)]),
            ],
            axis=dim,
        )
    return cells


def cheb_matrix(points):
    indices = np.arange(points)
    heights = (1.0 - np.cos(np.pi * indices / (points - 1))) / 2.0
    weights = np.where(indices % 2 == 0, 1.0, -1.0)
    weights[0] = weights[0] * 0.5
    weights[-1] = weights[-1] * 0.5
    identity = np.eye(points)
    spacing = heights[:, None] - heights[None, :] + identity
    matrix = weights[None, :] / weights[:, None] / spacing
    matrix = np.where(identity > 0.5, 0.0, matrix)
    matrix = matrix - identity * matrix.sum(axis=1)[:, None]
    return (matrix.astype(np.float32), heights.astype(np.float32))


def set_bounds(profiles, matched):
    point = jnp.arange(profiles.shape[1])[None, :, None, None]
    state = jnp.where(point == profiles.shape[1] - 1, matched[:, None], profiles)
    return jnp.where(point == 0, jnp.float32(0.0), state)


def advance(state, padded, burning, deriv, heights):
    grad = jnp.einsum("ij,kjrc->kirc", deriv, state, precision=lax.Precision.HIGHEST)
    shear = jnp.sqrt(grad[0] * grad[0] + grad[1] * grad[1] + 1e-06)
    visc = visc_base + mix_coef * (heights * heights)[:, None, None] * shear
    scales = jnp.array([1.0, 1.0, 1.0 / prandtl], jnp.float32)[:, None, None, None]
    diffusion = jnp.einsum(
        "ij,kjrc->kirc", deriv, visc[None] * scales * grad, precision=lax.Precision.HIGHEST
    )
    lateral = padded[:, :, 2:] + padded[:, :, :-2] - 2.0 * state
    source = burn_rate * jnp.exp(-heights / 0.15)[:, None, None] * burning.astype(jnp.float32)[None]
    tendency = diffusion + lateral_coef * lateral
    tendency = tendency.at[2].add(source)
    point = jnp.arange(state.shape[1])
    interior = ((point > 0) & (point < state.shape[1] - 1))[None, :, None, None]
    new_state = jnp.where(interior, state + step_size * tendency, state)
    stress = (
        visc_base
        * scales[:, 0]
        * jnp.einsum("j,kjrc->krc", deriv[0], new_state, precision=lax.Precision.HIGHEST)
    )
    return (new_state, stress)


def on_device(profiles, plane, match_cell, burning):
    normal_count = lax.axis_size("normal")
    deriv_np, height_np = cheb_matrix(profiles.shape[1])
    deriv = jnp.asarray(deriv_np, jnp.float32)
    heights = jnp.asarray(height_np, jnp.float32)
    face_rows, face_cols = (profiles.shape[2], profiles.shape[3])
    plane_rows, plane_cols = (plane.shape[1], plane.shape[2])
    cell_count = plane_rows * plane_cols
    wanted = (match_cell % cell_count).reshape(normal_count, -1)
    received = lax.all_to_all(wanted, "normal", split_axis=0, concat_axis=0, tiled=True)
    cells = received.reshape(-1)
    lanes = plane_cols // 8
    blocks = plane_cols // lanes
    lane_hot = (cells[:, None] % lanes == jnp.arange(lanes)[None, :]).astype(jnp.float32)
    tile = cells // lanes
    tile_order = (tile % blocks) * plane_rows + tile // blocks
    tile_hot = (jnp.arange(plane_rows * blocks)[:, None] == tile_order[None, :]).astype(jnp.float32)
    tiled_plane = (
        plane.reshape(3, plane_rows, blocks, lanes).transpose(0, 2, 1, 3).reshape(3, -1, lanes)
    )
    picked = jnp.einsum("khl,fl->khf", tiled_plane, lane_hot, precision=lax.Precision.HIGHEST)
    served = jnp.sum(picked * tile_hot[None], axis=1).reshape(3, normal_count, -1)
    matched = lax.all_to_all(served, "normal", split_axis=1, concat_axis=1, tiled=True).reshape(
        3, face_rows, face_cols
    )
    state = set_bounds(profiles, matched)
    padded = padded_2(profiles, (("wall", 2),), 1)
    new_state, stress = advance(state, padded, burning, deriv, heights)
    returned = lax.all_to_all(
        stress.reshape(3, normal_count, -1), "normal", split_axis=1, concat_axis=1, tiled=True
    )
    spread = returned.reshape(3, 1, -1) * tile_hot[None]
    summed = jnp.einsum("khf,fl->khl", spread, lane_hot, precision=lax.Precision.HIGHEST)
    wall_flux = summed.reshape(3, blocks, plane_rows, lanes).transpose(0, 2, 1, 3)
    return (new_state, wall_flux.reshape(plane.shape))


def solution(mesh):
    return jax.shard_map(
        on_device,
        mesh=mesh,
        in_specs=(
            P(None, None, "wall", "normal"),
            P(None, "wall", "normal"),
            P("wall", "normal"),
            P("wall", "normal"),
        ),
        out_specs=(P(None, None, "wall", "normal"), P(None, "wall", "normal")),
        check_vma=False,
    )
```

```python
import jax
import jax.numpy as jnp
import numpy as np
from jax import lax
from jax.sharding import PartitionSpec as P

visc_base = 0.001
mix_coef = 1e-05
prandtl = 0.7
burn_rate = 15000.0
lateral_coef = 4000.0
step_size = 2e-05


def padded_2(cells, sides, width):
    for axis, dim in sides:
        count = lax.axis_size(axis)
        ends = count - 1
        head = lax.slice_in_dim(cells, 0, width, axis=dim)
        tail = lax.slice_in_dim(cells, cells.shape[dim] - width, cells.shape[dim], axis=dim)
        cells = jnp.concatenate(
            [
                lax.ppermute(tail, axis, [(i, (i + 1) % count) for i in range(ends)]),
                cells,
                lax.ppermute(head, axis, [((i + 1) % count, i) for i in range(ends)]),
            ],
            axis=dim,
        )
    return cells


def cheb_matrix(points):
    indices = np.arange(points)
    heights = (1.0 - np.cos(np.pi * indices / (points - 1))) / 2.0
    weights = np.where(indices % 2 == 0, 1.0, -1.0)
    weights[0] = weights[0] * 0.5
    weights[-1] = weights[-1] * 0.5
    identity = np.eye(points)
    spacing = heights[:, None] - heights[None, :] + identity
    matrix = weights[None, :] / weights[:, None] / spacing
    matrix = np.where(identity > 0.5, 0.0, matrix)
    matrix = matrix - identity * matrix.sum(axis=1)[:, None]
    return (matrix.astype(np.float32), heights.astype(np.float32))


def set_bounds(profiles, matched):
    point = jnp.arange(profiles.shape[1])[None, :, None, None]
    state = jnp.where(point == profiles.shape[1] - 1, matched[:, None], profiles)
    return jnp.where(point == 0, jnp.float32(0.0), state)


def prepare(profiles, padded, burning, deriv, heights):
    point = jnp.arange(profiles.shape[1])
    interior = ((point > 0) & (point < profiles.shape[1] - 1))[None, :, None, None]
    inner = jnp.where(interior, profiles, jnp.float32(0.0))
    partial = jnp.einsum("ij,kjrc->kirc", deriv, inner, precision=lax.Precision.HIGHEST)
    lateral = padded[:, :, 2:] + padded[:, :, :-2] - 2.0 * profiles
    source = burn_rate * jnp.exp(-heights / 0.15)[:, None, None] * burning.astype(jnp.float32)[None]
    forcing = lateral_coef * lateral
    forcing = forcing.at[2].add(source)
    return (partial, forcing)


def advance(state, matched, partial, forcing, deriv, heights):
    grad = partial + deriv[:, -1][None, :, None, None] * matched[:, None]
    shear = jnp.sqrt(grad[0] * grad[0] + grad[1] * grad[1] + 1e-06)
    visc = visc_base + mix_coef * (heights * heights)[:, None, None] * shear
    scales = jnp.array([1.0, 1.0, 1.0 / prandtl], jnp.float32)[:, None, None, None]
    diffusion = jnp.einsum(
        "ij,kjrc->kirc", deriv, visc[None] * scales * grad, precision=lax.Precision.HIGHEST
    )
    tendency = diffusion + forcing
    point = jnp.arange(state.shape[1])
    interior = ((point > 0) & (point < state.shape[1] - 1))[None, :, None, None]
    new_state = jnp.where(interior, state + step_size * tendency, state)
    stress = (
        visc_base
        * scales[:, 0]
        * jnp.einsum("j,kjrc->krc", deriv[0], new_state, precision=lax.Precision.HIGHEST)
    )
    return (new_state, stress)


def on_device(profiles, plane, match_cell, burning):
    normal_count = lax.axis_size("normal")
    deriv_np, height_np = cheb_matrix(profiles.shape[1])
    deriv = jnp.asarray(deriv_np, jnp.float32)
    heights = jnp.asarray(height_np, jnp.float32)
    face_rows, face_cols = (profiles.shape[2], profiles.shape[3])
    plane_rows, plane_cols = (plane.shape[1], plane.shape[2])
    cell_count = plane_rows * plane_cols
    wanted = match_cell.reshape(normal_count, -1)
    received = lax.all_to_all(wanted, "normal", split_axis=0, concat_axis=0, tiled=True)
    cells = received.reshape(-1) % cell_count
    lanes = plane_cols // 8
    blocks = plane_cols // lanes
    lane_hot = (cells[:, None] % lanes == jnp.arange(lanes)[None, :]).astype(jnp.float32)
    tile = cells // lanes
    tile_order = (tile % blocks) * plane_rows + tile // blocks
    tile_hot = (jnp.arange(plane_rows * blocks)[:, None] == tile_order[None, :]).astype(jnp.float32)
    tiled_plane = (
        plane.reshape(3, plane_rows, blocks, lanes).transpose(0, 2, 1, 3).reshape(3, -1, lanes)
    )
    picked = jnp.einsum("khl,fl->khf", tiled_plane, lane_hot, precision=lax.Precision.HIGHEST)
    served = jnp.sum(picked * tile_hot[None], axis=1).reshape(3, normal_count, -1)
    served = served.transpose(1, 0, 2)
    padded = padded_2(profiles, (("wall", 2),), 1)
    partial, forcing = prepare(profiles, padded, burning, deriv, heights)
    served, partial, forcing = lax.optimization_barrier((served, partial, forcing))
    matched = lax.all_to_all(served, "normal", split_axis=0, concat_axis=0, tiled=True)
    matched = matched.transpose(1, 0, 2).reshape(3, face_rows, face_cols)
    state = set_bounds(profiles, matched)
    new_state, stress = advance(state, matched, partial, forcing, deriv, heights)
    returned = lax.all_to_all(
        stress.reshape(3, normal_count, -1).transpose(1, 0, 2),
        "normal",
        split_axis=0,
        concat_axis=0,
        tiled=True,
    ).transpose(1, 0, 2)
    spread = returned.reshape(3, 1, -1) * tile_hot[None]
    summed = jnp.einsum("khf,fl->khl", spread, lane_hot, precision=lax.Precision.HIGHEST)
    wall_flux = summed.reshape(3, blocks, plane_rows, lanes).transpose(0, 2, 1, 3)
    return (new_state, wall_flux.reshape(plane.shape))


def solution(mesh):
    return jax.shard_map(
        on_device,
        mesh=mesh,
        in_specs=(
            P(None, None, "wall", "normal"),
            P(None, "wall", "normal"),
            P("wall", "normal"),
            P("wall", "normal"),
        ),
        out_specs=(P(None, None, "wall", "normal"), P(None, "wall", "normal")),
        check_vma=False,
    )
```

```python
import jax
import jax.numpy as jnp
import numpy as np
from jax import lax
from jax.sharding import PartitionSpec as P

visc_base = 0.001
mix_coef = 1e-05
prandtl = 0.7
burn_rate = 15000.0
lateral_coef = 4000.0
step_size = 2e-05


def padded_2(cells, sides, width):
    for axis, dim in sides:
        count = lax.axis_size(axis)
        ends = count - 1
        head = lax.slice_in_dim(cells, 0, width, axis=dim)
        tail = lax.slice_in_dim(cells, cells.shape[dim] - width, cells.shape[dim], axis=dim)
        cells = jnp.concatenate(
            [
                lax.ppermute(tail, axis, [(i, (i + 1) % count) for i in range(ends)]),
                cells,
                lax.ppermute(head, axis, [((i + 1) % count, i) for i in range(ends)]),
            ],
            axis=dim,
        )
    return cells


def cheb_matrix(points):
    indices = np.arange(points)
    heights = (1.0 - np.cos(np.pi * indices / (points - 1))) / 2.0
    weights = np.where(indices % 2 == 0, 1.0, -1.0)
    weights[0] = weights[0] * 0.5
    weights[-1] = weights[-1] * 0.5
    identity = np.eye(points)
    spacing = heights[:, None] - heights[None, :] + identity
    matrix = weights[None, :] / weights[:, None] / spacing
    matrix = np.where(identity > 0.5, 0.0, matrix)
    matrix = matrix - identity * matrix.sum(axis=1)[:, None]
    return (matrix.astype(np.float32), heights.astype(np.float32))


def set_bounds(profiles, matched):
    point = jnp.arange(profiles.shape[1])[None, :, None, None]
    state = jnp.where(point == profiles.shape[1] - 1, matched[:, None], profiles)
    return jnp.where(point == 0, jnp.float32(0.0), state)


def prepare(profiles, padded, burning, heights):
    lateral = padded[:, :, 2:] + padded[:, :, :-2] - 2.0 * profiles
    source = burn_rate * jnp.exp(-heights / 0.15)[:, None, None] * burning.astype(jnp.float32)[None]
    forcing = lateral_coef * lateral
    forcing = forcing.at[2].add(source)
    return forcing


def advance(state, matched, partial, forcing, deriv, heights):
    grad = partial + deriv[:, -1][None, :, None, None] * matched[:, None]
    shear = jnp.sqrt(grad[0] * grad[0] + grad[1] * grad[1] + 1e-06)
    visc = visc_base + mix_coef * (heights * heights)[:, None, None] * shear
    scales = jnp.where(jnp.arange(3) == 2, jnp.float32(1.0 / prandtl), jnp.float32(1.0))
    scales = scales[:, None, None, None]
    diffusion = jnp.einsum(
        "ij,kjrc->kirc", deriv, visc[None] * scales * grad, precision=lax.Precision.HIGHEST
    )
    tendency = diffusion + forcing
    point = jnp.arange(state.shape[1])
    interior = ((point > 0) & (point < state.shape[1] - 1))[None, :, None, None]
    new_state = jnp.where(interior, state + step_size * tendency, state)
    stress = (
        visc_base
        * scales[:, 0]
        * jnp.einsum("j,kjrc->krc", deriv[0], new_state, precision=lax.Precision.HIGHEST)
    )
    return (new_state, stress)


def on_device(profiles, plane, match_cell, burning):
    normal_count = lax.axis_size("normal")
    deriv_np, height_np = cheb_matrix(profiles.shape[1])
    table = jnp.asarray(np.concatenate([deriv_np, height_np[None, :]], axis=0), jnp.float32)
    table = lax.optimization_barrier(table)
    deriv = table[:-1]
    heights = table[-1]
    face_rows, face_cols = (profiles.shape[2], profiles.shape[3])
    plane_rows, plane_cols = (plane.shape[1], plane.shape[2])
    cell_count = plane_rows * plane_cols
    wanted = match_cell.reshape(normal_count, -1)
    received = lax.all_to_all(wanted, "normal", split_axis=0, concat_axis=0, tiled=True)
    point = jnp.arange(profiles.shape[1])
    interior = ((point > 0) & (point < profiles.shape[1] - 1))[None, :, None, None]
    inner = jnp.where(interior, profiles, jnp.float32(0.0))
    partial = jnp.einsum("ij,kjrc->kirc", deriv, inner, precision=lax.Precision.HIGHEST)
    partial, inner, received = lax.optimization_barrier((partial, inner, received))
    cells = received.reshape(-1) % cell_count
    lanes = plane_cols // 8
    blocks = plane_cols // lanes
    lane_hot = (cells[:, None] % lanes == jnp.arange(lanes)[None, :]).astype(jnp.float32)
    tile = cells // lanes
    tile_order = (tile % blocks) * plane_rows + tile // blocks
    tile_hot = (jnp.arange(plane_rows * blocks)[:, None] == tile_order[None, :]).astype(jnp.float32)
    tiled_plane = (
        plane.reshape(3, plane_rows, blocks, lanes).transpose(0, 2, 1, 3).reshape(3, -1, lanes)
    )
    picked = jnp.einsum("khl,fl->khf", tiled_plane, lane_hot, precision=lax.Precision.HIGHEST)
    served = jnp.sum(picked * tile_hot[None], axis=1).reshape(3, normal_count, -1)
    served = served.transpose(1, 0, 2)
    edges, served = lax.optimization_barrier((inner, served))
    padded = padded_2(edges, (("wall", 2),), 1)
    forcing = prepare(inner, padded, burning, heights)
    matched = lax.all_to_all(served, "normal", split_axis=0, concat_axis=0, tiled=True)
    matched = matched.transpose(1, 0, 2).reshape(3, face_rows, face_cols)
    state = set_bounds(profiles, matched)
    new_state, stress = advance(state, matched, partial, forcing, deriv, heights)
    returned = lax.all_to_all(
        stress.reshape(3, normal_count, -1).transpose(1, 0, 2),
        "normal",
        split_axis=0,
        concat_axis=0,
        tiled=True,
    ).transpose(1, 0, 2)
    spread = returned.reshape(3, 1, -1) * tile_hot[None]
    summed = jnp.einsum("khf,fl->khl", spread, lane_hot, precision=lax.Precision.HIGHEST)
    wall_flux = summed.reshape(3, blocks, plane_rows, lanes).transpose(0, 2, 1, 3)
    return (new_state, wall_flux.reshape(plane.shape))


def solution(mesh):
    return jax.shard_map(
        on_device,
        mesh=mesh,
        in_specs=(
            P(None, None, "wall", "normal"),
            P(None, "wall", "normal"),
            P("wall", "normal"),
            P("wall", "normal"),
        ),
        out_specs=(P(None, None, "wall", "normal"), P(None, "wall", "normal")),
        check_vma=False,
    )
```

```python
import jax
import jax.numpy as jnp
import numpy as np
from jax import lax
from jax.sharding import PartitionSpec as P

visc_base = 0.001
mix_coef = 1e-05
prandtl = 0.7
burn_rate = 15000.0
lateral_coef = 4000.0
step_size = 2e-05


def padded_2(cells, sides, width):
    for axis, dim in sides:
        count = lax.axis_size(axis)
        ends = count - 1
        head = lax.slice_in_dim(cells, 0, width, axis=dim)
        tail = lax.slice_in_dim(cells, cells.shape[dim] - width, cells.shape[dim], axis=dim)
        cells = jnp.concatenate(
            [
                lax.ppermute(tail, axis, [(i, (i + 1) % count) for i in range(ends)]),
                cells,
                lax.ppermute(head, axis, [((i + 1) % count, i) for i in range(ends)]),
            ],
            axis=dim,
        )
    return cells


def cheb_matrix(points):
    indices = np.arange(points)
    heights = (1.0 - np.cos(np.pi * indices / (points - 1))) / 2.0
    weights = np.where(indices % 2 == 0, 1.0, -1.0)
    weights[0] = weights[0] * 0.5
    weights[-1] = weights[-1] * 0.5
    identity = np.eye(points)
    spacing = heights[:, None] - heights[None, :] + identity
    matrix = weights[None, :] / weights[:, None] / spacing
    matrix = np.where(identity > 0.5, 0.0, matrix)
    matrix = matrix - identity * matrix.sum(axis=1)[:, None]
    return (matrix.astype(np.float32), heights.astype(np.float32))


def set_bounds(profiles, matched):
    point = jnp.arange(profiles.shape[1])[None, :, None, None]
    state = jnp.where(point == profiles.shape[1] - 1, matched[:, None], profiles)
    return jnp.where(point == 0, jnp.float32(0.0), state)


def advance(state, padded, burning, deriv, heights):
    grad = jnp.einsum("ij,kjrc->kirc", deriv, state, precision=lax.Precision.HIGHEST)
    shear = jnp.sqrt(grad[0] * grad[0] + grad[1] * grad[1] + 1e-06)
    visc = visc_base + mix_coef * (heights * heights)[:, None, None] * shear
    scales = jnp.where(jnp.arange(3) == 2, jnp.float32(1.0 / prandtl), jnp.float32(1.0))
    scales = scales[:, None, None, None]
    diffusion = jnp.einsum(
        "ij,kjrc->kirc", deriv, visc[None] * scales * grad, precision=lax.Precision.HIGHEST
    )
    lateral = padded[:, :, 2:] + padded[:, :, :-2] - 2.0 * state
    source = burn_rate * jnp.exp(-heights / 0.15)[:, None, None] * burning.astype(jnp.float32)[None]
    tendency = diffusion + lateral_coef * lateral
    tendency = tendency.at[2].add(source)
    point = jnp.arange(state.shape[1])
    interior = ((point > 0) & (point < state.shape[1] - 1))[None, :, None, None]
    new_state = jnp.where(interior, state + step_size * tendency, state)
    stress = (
        visc_base
        * scales[:, 0]
        * jnp.einsum("j,kjrc->krc", deriv[0], new_state, precision=lax.Precision.HIGHEST)
    )
    return (new_state, stress)


def on_device(profiles, plane, match_cell, burning):
    normal_count = lax.axis_size("normal")
    deriv_np, height_np = cheb_matrix(profiles.shape[1])
    table = jnp.asarray(np.concatenate([deriv_np, height_np[None, :]], axis=0), jnp.float32)
    table = lax.optimization_barrier(table)
    deriv = table[:-1]
    heights = table[-1]
    face_rows, face_cols = (profiles.shape[2], profiles.shape[3])
    plane_rows, plane_cols = (plane.shape[1], plane.shape[2])
    cell_count = plane_rows * plane_cols
    wanted = match_cell.reshape(normal_count, -1)
    received = lax.all_to_all(wanted, "normal", split_axis=0, concat_axis=0, tiled=True)
    received = lax.optimization_barrier(received)
    cells = received.reshape(-1) % cell_count
    lanes = plane_cols // 8
    blocks = plane_cols // lanes
    lane_hot = (cells[:, None] % lanes == jnp.arange(lanes)[None, :]).astype(jnp.float32)
    tile = cells // lanes
    tile_order = (tile % blocks) * plane_rows + tile // blocks
    tile_hot = (jnp.arange(plane_rows * blocks)[:, None] == tile_order[None, :]).astype(jnp.float32)
    tiled_plane = (
        plane.reshape(3, plane_rows, blocks, lanes).transpose(0, 2, 1, 3).reshape(3, -1, lanes)
    )
    picked = jnp.einsum("khl,fl->khf", tiled_plane, lane_hot, precision=lax.Precision.HIGHEST)
    served = jnp.sum(picked * tile_hot[None], axis=1).reshape(3, normal_count, -1)
    matched = lax.all_to_all(served, "normal", split_axis=1, concat_axis=1, tiled=True).reshape(
        3, face_rows, face_cols
    )
    state = set_bounds(profiles, matched)
    padded = padded_2(profiles, (("wall", 2),), 1)
    new_state, stress = advance(state, padded, burning, deriv, heights)
    returned = lax.all_to_all(
        stress.reshape(3, normal_count, -1), "normal", split_axis=1, concat_axis=1, tiled=True
    )
    spread = returned.reshape(3, 1, -1) * tile_hot[None]
    summed = jnp.einsum("khf,fl->khl", spread, lane_hot, precision=lax.Precision.HIGHEST)
    wall_flux = summed.reshape(3, blocks, plane_rows, lanes).transpose(0, 2, 1, 3)
    return (new_state, wall_flux.reshape(plane.shape))


def solution(mesh):
    return jax.shard_map(
        on_device,
        mesh=mesh,
        in_specs=(
            P(None, None, "wall", "normal"),
            P(None, "wall", "normal"),
            P("wall", "normal"),
            P("wall", "normal"),
        ),
        out_specs=(P(None, None, "wall", "normal"), P(None, "wall", "normal")),
        check_vma=False,
    )
```

```python
import jax
import jax.numpy as jnp
import numpy as np
from jax import lax
from jax.experimental import pallas as pl
from jax.experimental.pallas import tpu as pltpu
from jax.sharding import PartitionSpec as P

visc_base = 0.001
mix_coef = 1e-05
prandtl = 0.7
burn_rate = 15000.0
lateral_coef = 4000.0
step_size = 2e-05


def padded_2(cells, sides, width):
    for axis, dim in sides:
        count = lax.axis_size(axis)
        ends = count - 1
        head = lax.slice_in_dim(cells, 0, width, axis=dim)
        tail = lax.slice_in_dim(cells, cells.shape[dim] - width, cells.shape[dim], axis=dim)
        cells = jnp.concatenate(
            [
                lax.ppermute(tail, axis, [(i, (i + 1) % count) for i in range(ends)]),
                cells,
                lax.ppermute(head, axis, [((i + 1) % count, i) for i in range(ends)]),
            ],
            axis=dim,
        )
    return cells


def cheb_matrix(points):
    indices = np.arange(points)
    heights = (1.0 - np.cos(np.pi * indices / (points - 1))) / 2.0
    weights = np.where(indices % 2 == 0, 1.0, -1.0)
    weights[0] = weights[0] * 0.5
    weights[-1] = weights[-1] * 0.5
    identity = np.eye(points)
    spacing = heights[:, None] - heights[None, :] + identity
    matrix = weights[None, :] / weights[:, None] / spacing
    matrix = np.where(identity > 0.5, 0.0, matrix)
    matrix = matrix - identity * matrix.sum(axis=1)[:, None]
    return (matrix.astype(np.float32), heights.astype(np.float32))


def set_bounds(profiles, matched):
    point = jnp.arange(profiles.shape[1])[None, :, None, None]
    state = jnp.where(point == profiles.shape[1] - 1, matched[:, None], profiles)
    return jnp.where(point == 0, jnp.float32(0.0), state)


def advance(state, padded, burning, deriv, heights):
    grad = jnp.einsum("ij,kjrc->kirc", deriv, state, precision=lax.Precision.HIGHEST)
    shear = jnp.sqrt(grad[0] * grad[0] + grad[1] * grad[1] + 1e-06)
    visc = visc_base + mix_coef * (heights * heights)[:, None, None] * shear
    scales = jnp.where(jnp.arange(3) == 2, jnp.float32(1.0 / prandtl), jnp.float32(1.0))
    scales = scales[:, None, None, None]
    diffusion = jnp.einsum(
        "ij,kjrc->kirc", deriv, visc[None] * scales * grad, precision=lax.Precision.HIGHEST
    )
    lateral = padded[:, :, 2:] + padded[:, :, :-2] - 2.0 * state
    source = burn_rate * jnp.exp(-heights / 0.15)[:, None, None] * burning.astype(jnp.float32)[None]
    tendency = diffusion + lateral_coef * lateral
    tendency = tendency.at[2].add(source)
    point = jnp.arange(state.shape[1])
    interior = ((point > 0) & (point < state.shape[1] - 1))[None, :, None, None]
    new_state = jnp.where(interior, state + step_size * tendency, state)
    stress = (
        visc_base
        * scales[:, 0]
        * jnp.einsum("j,kjrc->krc", deriv[0], new_state, precision=lax.Precision.HIGHEST)
    )
    return (new_state, stress)


def step_kernel(prof_ref, up_ref, down_ref, matched_ref, burn_ref, table_ref, new_ref, stress_ref):
    points = prof_ref.shape[2]
    deriv = table_ref[:points, :]
    heights = table_ref[points:, :].reshape(points, 1)
    row = lax.broadcasted_iota(jnp.int32, (points, 1), 0)
    interior = (row > 0) & (row < points - 1)
    lift = mix_coef * heights * heights
    burn_profile = burn_rate * jnp.exp(-heights / 0.15)
    first = deriv[0:1, :]
    hp = lax.Precision.HIGHEST
    for r in range(prof_ref.shape[1]):
        states = []
        grads = []
        for k in range(3):
            top = matched_ref[k, r : r + 1, :]
            state = jnp.where(row == points - 1, top, prof_ref[k, r])
            state = jnp.where(row == 0, jnp.float32(0.0), state)
            states.append(state)
            grads.append(jnp.dot(deriv, state, precision=hp, preferred_element_type=jnp.float32))
        shear = jnp.sqrt(grads[0] * grads[0] + grads[1] * grads[1] + 1e-06)
        visc = visc_base + lift * shear
        for k in range(3):
            scale = 1.0 / prandtl if k == 2 else 1.0
            diffusion = jnp.dot(
                deriv, visc * jnp.float32(scale) * grads[k], precision=hp,
                preferred_element_type=jnp.float32,
            )
            above = up_ref[k] if r == 0 else prof_ref[k, r - 1]
            below = down_ref[k] if r == prof_ref.shape[1] - 1 else prof_ref[k, r + 1]
            lateral = below + above - 2.0 * states[k]
            tendency = diffusion + lateral_coef * lateral
            if k == 2:
                tendency = tendency + burn_profile * burn_ref[r : r + 1, :]
            new = jnp.where(interior, states[k] + step_size * tendency, states[k])
            new_ref[k, r] = new
            slope = jnp.dot(first, new, precision=hp, preferred_element_type=jnp.float32)
            stress_ref[k, r : r + 1, :] = visc_base * jnp.float32(scale) * slope


def face_step(prof_t, up, down, matched, burning, table):
    k, rows, points, cols = prof_t.shape
    return pl.pallas_call(
        step_kernel,
        out_shape=(
            jax.ShapeDtypeStruct(prof_t.shape, jnp.float32),
            jax.ShapeDtypeStruct((k, rows, cols), jnp.float32),
        ),
        in_specs=[pl.BlockSpec(memory_space=pltpu.VMEM)] * 6,
        out_specs=(pl.BlockSpec(memory_space=pltpu.VMEM), pl.BlockSpec(memory_space=pltpu.VMEM)),
        cost_estimate=pl.CostEstimate(
            flops=4 * k * rows * points * points * cols * 6,
            bytes_accessed=4 * (4 * k * rows * points * cols),
            transcendentals=rows * points * cols,
        ),
    )(prof_t, up, down, matched, burning, table)


def on_device(profiles, plane, match_cell, burning):
    normal_count = lax.axis_size("normal")
    deriv_np, height_np = cheb_matrix(profiles.shape[1])
    table = jnp.asarray(np.concatenate([deriv_np, height_np[None, :]], axis=0), jnp.float32)
    table = lax.optimization_barrier(table)
    deriv = table[:-1]
    heights = table[-1]
    face_rows, face_cols = (profiles.shape[2], profiles.shape[3])
    plane_rows, plane_cols = (plane.shape[1], plane.shape[2])
    cell_count = plane_rows * plane_cols
    wanted = match_cell.reshape(normal_count, -1)
    received = lax.all_to_all(wanted, "normal", split_axis=0, concat_axis=0, tiled=True)
    received = lax.optimization_barrier(received)
    cells = received.reshape(-1) % cell_count
    lanes = plane_cols // 8
    blocks = plane_cols // lanes
    lane_hot = (cells[:, None] % lanes == jnp.arange(lanes)[None, :]).astype(jnp.float32)
    tile = cells // lanes
    tile_order = (tile % blocks) * plane_rows + tile // blocks
    tile_hot = (jnp.arange(plane_rows * blocks)[:, None] == tile_order[None, :]).astype(jnp.float32)
    tiled_plane = (
        plane.reshape(3, plane_rows, blocks, lanes).transpose(0, 2, 1, 3).reshape(3, -1, lanes)
    )
    picked = jnp.einsum("khl,fl->khf", tiled_plane, lane_hot, precision=lax.Precision.HIGHEST)
    served = jnp.sum(picked * tile_hot[None], axis=1).reshape(3, normal_count, -1)
    matched = lax.all_to_all(served, "normal", split_axis=1, concat_axis=1, tiled=True).reshape(
        3, face_rows, face_cols
    )
    count = lax.axis_size("wall")
    head = profiles[:, :, :1]
    tail = profiles[:, :, -1:]
    up = lax.ppermute(tail, "wall", [(i, i + 1) for i in range(count - 1)])[:, :, 0]
    down = lax.ppermute(head, "wall", [(i + 1, i) for i in range(count - 1)])[:, :, 0]
    new_t, stress = face_step(
        profiles.transpose(0, 2, 1, 3), up, down, matched, burning.astype(jnp.float32), table
    )
    new_state = new_t.transpose(0, 2, 1, 3)
    returned = lax.all_to_all(
        stress.reshape(3, normal_count, -1), "normal", split_axis=1, concat_axis=1, tiled=True
    )
    spread = returned.reshape(3, 1, -1) * tile_hot[None]
    summed = jnp.einsum("khf,fl->khl", spread, lane_hot, precision=lax.Precision.HIGHEST)
    wall_flux = summed.reshape(3, blocks, plane_rows, lanes).transpose(0, 2, 1, 3)
    return (new_state, wall_flux.reshape(plane.shape))


def solution(mesh):
    return jax.shard_map(
        on_device,
        mesh=mesh,
        in_specs=(
            P(None, None, "wall", "normal"),
            P(None, "wall", "normal"),
            P("wall", "normal"),
            P("wall", "normal"),
        ),
        out_specs=(P(None, None, "wall", "normal"), P(None, "wall", "normal")),
        check_vma=False,
    )
```

```python
import jax
import jax.numpy as jnp
import numpy as np
from jax import lax
from jax.sharding import PartitionSpec as P

visc_base = 0.001
mix_coef = 1e-05
prandtl = 0.7
burn_rate = 15000.0
lateral_coef = 4000.0
step_size = 2e-05


def padded_2(cells, sides, width):
    for axis, dim in sides:
        count = lax.axis_size(axis)
        ends = count - 1
        head = lax.slice_in_dim(cells, 0, width, axis=dim)
        tail = lax.slice_in_dim(cells, cells.shape[dim] - width, cells.shape[dim], axis=dim)
        cells = jnp.concatenate(
            [
                lax.ppermute(tail, axis, [(i, (i + 1) % count) for i in range(ends)]),
                cells,
                lax.ppermute(head, axis, [((i + 1) % count, i) for i in range(ends)]),
            ],
            axis=dim,
        )
    return cells


def edge_padded(cells, head, tail, axis):
    count = lax.axis_size(axis)
    above = lax.ppermute(tail, axis, [(i, i + 1) for i in range(count - 1)])
    below = lax.ppermute(head, axis, [(i + 1, i) for i in range(count - 1)])
    return jnp.concatenate([above, cells, below], axis=2)


def cheb_matrix(points):
    indices = np.arange(points)
    heights = (1.0 - np.cos(np.pi * indices / (points - 1))) / 2.0
    weights = np.where(indices % 2 == 0, 1.0, -1.0)
    weights[0] = weights[0] * 0.5
    weights[-1] = weights[-1] * 0.5
    identity = np.eye(points)
    spacing = heights[:, None] - heights[None, :] + identity
    matrix = weights[None, :] / weights[:, None] / spacing
    matrix = np.where(identity > 0.5, 0.0, matrix)
    matrix = matrix - identity * matrix.sum(axis=1)[:, None]
    return (matrix.astype(np.float32), heights.astype(np.float32))


def set_bounds(profiles, matched):
    point = jnp.arange(profiles.shape[1])[None, :, None, None]
    state = jnp.where(point == profiles.shape[1] - 1, matched[:, None], profiles)
    return jnp.where(point == 0, jnp.float32(0.0), state)


def advance(state, padded, burning, deriv, heights):
    grad = jnp.einsum("ij,kjrc->kirc", deriv, state, precision=lax.Precision.HIGHEST)
    shear = jnp.sqrt(grad[0] * grad[0] + grad[1] * grad[1] + 1e-06)
    visc = visc_base + mix_coef * (heights * heights)[:, None, None] * shear
    scales = jnp.where(jnp.arange(3) == 2, jnp.float32(1.0 / prandtl), jnp.float32(1.0))
    scales = scales[:, None, None, None]
    diffusion = jnp.einsum(
        "ij,kjrc->kirc", deriv, visc[None] * scales * grad, precision=lax.Precision.HIGHEST
    )
    lateral = padded[:, :, 2:] + padded[:, :, :-2] - 2.0 * state
    source = burn_rate * jnp.exp(-heights / 0.15)[:, None, None] * burning.astype(jnp.float32)[None]
    tendency = diffusion + lateral_coef * lateral
    tendency = tendency.at[2].add(source)
    point = jnp.arange(state.shape[1])
    interior = ((point > 0) & (point < state.shape[1] - 1))[None, :, None, None]
    new_state = jnp.where(interior, state + step_size * tendency, state)
    stress = (
        visc_base
        * scales[:, 0]
        * jnp.einsum("j,kjrc->krc", deriv[0], new_state, precision=lax.Precision.HIGHEST)
    )
    return (new_state, stress)


def on_device(profiles, plane, match_cell, burning):
    normal_count = lax.axis_size("normal")
    deriv_np, height_np = cheb_matrix(profiles.shape[1])
    table = jnp.asarray(np.concatenate([deriv_np, height_np[None, :]], axis=0), jnp.float32)
    table = lax.optimization_barrier(table)
    deriv = table[:-1]
    heights = table[-1]
    face_rows, face_cols = (profiles.shape[2], profiles.shape[3])
    plane_rows, plane_cols = (plane.shape[1], plane.shape[2])
    cell_count = plane_rows * plane_cols
    head, tail, match_cell = lax.optimization_barrier(
        (profiles[:, :, :1], profiles[:, :, -1:], match_cell)
    )
    wanted = match_cell.reshape(normal_count, -1)
    received = lax.all_to_all(wanted, "normal", split_axis=0, concat_axis=0, tiled=True)
    received = lax.optimization_barrier(received)
    cells = received.reshape(-1) % cell_count
    lanes = plane_cols // 8
    blocks = plane_cols // lanes
    lane_hot = (cells[:, None] % lanes == jnp.arange(lanes)[None, :]).astype(jnp.float32)
    tile = cells // lanes
    tile_order = (tile % blocks) * plane_rows + tile // blocks
    tile_hot = (jnp.arange(plane_rows * blocks)[:, None] == tile_order[None, :]).astype(jnp.float32)
    tiled_plane = (
        plane.reshape(3, plane_rows, blocks, lanes).transpose(0, 2, 1, 3).reshape(3, -1, lanes)
    )
    picked = jnp.einsum("khl,fl->khf", tiled_plane, lane_hot, precision=lax.Precision.HIGHEST)
    served = jnp.sum(picked * tile_hot[None], axis=1).reshape(3, normal_count, -1)
    matched = lax.all_to_all(served, "normal", split_axis=1, concat_axis=1, tiled=True).reshape(
        3, face_rows, face_cols
    )
    state = set_bounds(profiles, matched)
    padded = edge_padded(profiles, head, tail, "wall")
    new_state, stress = advance(state, padded, burning, deriv, heights)
    returned = lax.all_to_all(
        stress.reshape(3, normal_count, -1), "normal", split_axis=1, concat_axis=1, tiled=True
    )
    spread = returned.reshape(3, 1, -1) * tile_hot[None]
    summed = jnp.einsum("khf,fl->khl", spread, lane_hot, precision=lax.Precision.HIGHEST)
    wall_flux = summed.reshape(3, blocks, plane_rows, lanes).transpose(0, 2, 1, 3)
    return (new_state, wall_flux.reshape(plane.shape))


def solution(mesh):
    return jax.shard_map(
        on_device,
        mesh=mesh,
        in_specs=(
            P(None, None, "wall", "normal"),
            P(None, "wall", "normal"),
            P("wall", "normal"),
            P("wall", "normal"),
        ),
        out_specs=(P(None, None, "wall", "normal"), P(None, "wall", "normal")),
        check_vma=False,
    )
```
